256 devices in a mesh: adapter: 32 (over y, z), tensor: 8 (over x, core).
Axes of the slice: x: 4, y: 4, z: 8, core: 2. Of those that a mesh axis runs over, the one named last changes fastest.
Arguments:
- hidden_rows: bfloat16 [32768, 8192], P('adapter', 'tensor'), may hold values from -6 to 6
- kv_weight: bfloat16 [8192, 2, 1024], P(None, None, 'tensor'), may hold values from -0.0625 to 0.0625
- adapter_down: bfloat16 [512, 8192, 128], P('adapter', 'tensor'), may hold values from -0.0625 to 0.0625
- adapter_up: bfloat16 [512, 2, 64, 1024], P('adapter', None, None, 'tensor'), may hold values from -0.75 to 0.75
- adapter_ids: int32 [256], P('adapter'), may hold values from 0 to 511, as said below
Outputs:
- kv_out: bfloat16 [32768, 2, 1024], P('adapter', None, 'tensor')
The draws below stay inside these ranges and needn't reach their ends.
Inputs may be any that keep to these rules, and one draw needn't show every extreme that they name: `adapter_ids`: the adapters of the 8 blocks of one index of adapter have 8 different owners, the owner of adapter a being a // 16; some owners are named by far more devices than others.
All inputs are finite; a program needn't handle non-finite values.
Results may differ from the reference program's by a relative error of at most 0.005.
Values may be sent and summed in bfloat16 or wider, within the bound.
No kernel may reach another device: no remote copies, remote signals or barrier semaphores. Data moves between devices by JAX's collectives and lax.ppermute only.
A program may use at most 128 MiB of HBM per device.

```python
import jax
import jax.numpy as jnp
from jax import lax

D = 8192
KVH = 8
HD = 128
R = 64
BLOCK_ROWS = 128
BLOCKS_PER_UNIT = 8
ADAPT_DEV = 16
ROWS = 32768
BLOCKS = 256
ADAPTERS = 512


def draw_adapter_ids(key, part):
    holder_count = ADAPTERS // ADAPT_DEV
    group_total = BLOCKS // BLOCKS_PER_UNIT
    key_hot, key_score, key_order, key_local = jax.random.split(jax.random.fold_in(key, 17), 4)
    rank_order = jax.random.permutation(key_hot, holder_count)
    extra_credit = jnp.where(rank_order < min(2, BLOCKS_PER_UNIT), 1 << 28, 0).astype(jnp.int32)
    block_scores = jax.random.randint(key_score, (group_total, holder_count), 0, 1 << 16, dtype=jnp.int32)
    block_scores = block_scores * holder_count + jnp.arange(holder_count, dtype=jnp.int32)[None, :] + extra_credit[None, :]
    top_scores, chosen = lax.top_k(block_scores, BLOCKS_PER_UNIT)
    order_keys = jax.random.randint(key_order, (group_total, BLOCKS_PER_UNIT), 0, 1 << 16, dtype=jnp.int32)
    order_keys = order_keys * BLOCKS_PER_UNIT + jnp.arange(BLOCKS_PER_UNIT, dtype=jnp.int32)[None, :]
    ordering = jnp.argsort(order_keys, axis=1, stable=True)
    chosen = jnp.take_along_axis(chosen.astype(jnp.int32), ordering, axis=1)
    local_pick = jax.random.randint(key_local, (group_total, BLOCKS_PER_UNIT), 0, ADAPT_DEV, dtype=jnp.int32)
    return (chosen * ADAPT_DEV + local_pick).reshape(BLOCKS).astype(jnp.int32)


def steps_of(own_key, dims, cuts, low, largest):
    level = 1.0
    for position, parts in cuts:
        draws = jax.random.uniform(jax.random.fold_in(jax.random.fold_in(own_key, 6), position), (parts,), jnp.float32, low / len(cuts), largest / len(cuts))
        level = level * jnp.repeat(jnp.exp(draws), dims[position] // parts).reshape((-1,) + (1,) * (len(dims) - 1 - position))
    return level


def normal_values(own_key, dims, deviation, limit, pieces=(), held_as=jnp.bfloat16):
    values = jax.random.normal(own_key, dims, jnp.float32) * deviation
    if len(pieces) > 0:
        values = steps_of(own_key, dims, pieces, -0.22, 0.18) * values
    return jnp.clip(values, min=-limit, max=limit).astype(held_as)


def setup_inputs(seed: int = 0) -> dict:
    arg_keys = jax.random.split(jax.random.key(seed), 6)
    hidden_rows = normal_values(arg_keys[0], (ROWS, D), 1.0, 6.0, ((0, 32), (1, 8)))
    kv_weight = normal_values(arg_keys[1], (D, 2, KVH * HD), D ** -0.5, 0.0625, ((2, 8),))
    adapter_down = normal_values(arg_keys[2], (ADAPTERS, D, 2 * R), D ** -0.5, 0.0625, ((0, 32), (1, 8)))
    adapter_up = normal_values(arg_keys[3], (ADAPTERS, 2, R, KVH * HD), R ** -0.5, 0.75, ((0, 32), (3, 8)))
    adapter_ids = draw_adapter_ids(jax.random.fold_in(arg_keys[5], 71), 0)
    return {"hidden_rows": hidden_rows, "kv_weight": kv_weight, "adapter_down": adapter_down, "adapter_up": adapter_up, "adapter_ids": adapter_ids}


def reference(hidden_rows, kv_weight, adapter_down, adapter_up, adapter_ids):
    flat_weight = kv_weight.reshape(D, 2 * KVH * HD)
    base_out = jnp.dot(hidden_rows, flat_weight, preferred_element_type=jnp.float32).reshape(ROWS, 2, KVH * HD)
    row_blocks = hidden_rows.reshape(BLOCKS, BLOCK_ROWS, D)

    def single_block(pair):
        block_input, which = pair
        middle = jnp.dot(block_input, adapter_down[which], preferred_element_type=jnp.float32).astype(jnp.bfloat16)
        middle_split = middle.reshape(BLOCK_ROWS, 2, R).astype(jnp.float32)
        up_part = adapter_up[which].astype(jnp.float32)
        return jnp.einsum("rpk,pkh->rph", middle_split, up_part).astype(jnp.bfloat16)

    delta_rows = lax.map(single_block, (row_blocks, adapter_ids))
    summed = base_out + delta_rows.reshape(ROWS, 2, KVH * HD).astype(jnp.float32)
    return summed.astype(jnp.bfloat16)
```

```python
import jax
import jax.numpy as jnp
from jax import lax
from jax.sharding import PartitionSpec as P


def local(hidden_rows, kv_weight, adapter_down, adapter_up, adapter_ids):
    row_count, shard_width = hidden_rows.shape
    heads_local = kv_weight.shape[2]
    groups = lax.axis_size("adapter")
    owner_self = lax.axis_index("adapter")
    per_owner = adapter_down.shape[0]
    block_total = adapter_ids.shape[0]
    block_rows = row_count // block_total
    rank_size = adapter_up.shape[2]

    all_ids = lax.all_gather(adapter_ids, "adapter", axis=0, tiled=True)
    id_table = all_ids.reshape(groups, block_total)
    is_mine = id_table // per_owner == owner_self
    local_ids = jnp.sum(jnp.where(is_mine, id_table - owner_self * per_owner, 0), axis=1)

    feat_local = adapter_down.shape[1]
    up_rows = adapter_up.reshape(per_owner, 2 * rank_size, heads_local)
    send = jnp.concatenate([adapter_down[local_ids], up_rows[local_ids]], axis=1)
    received = lax.all_to_all(send, "adapter", split_axis=0, concat_axis=0, tiled=True)

    my_owners = adapter_ids // per_owner
    picked = received[my_owners]
    down_sel = picked[:, :feat_local]
    up_sel = picked[:, feat_local:].reshape(block_total, 2, rank_size, heads_local)

    row_blocks = hidden_rows.reshape(block_total, block_rows, shard_width)
    partial_value = jnp.einsum(
        "brd,bdk->brk", row_blocks, down_sel, preferred_element_type=jnp.float32
    )
    middle = lax.psum(partial_value, "tensor").astype(jnp.bfloat16)
    middle_split = middle.reshape(block_total, block_rows, 2, rank_size)
    delta_rows = jnp.einsum(
        "brpk,bpkh->brph", middle_split, up_sel, preferred_element_type=jnp.float32
    ).astype(jnp.bfloat16)

    flat_weight = kv_weight.reshape(kv_weight.shape[0], 2 * heads_local)
    base_out = jnp.dot(
        lax.all_gather(hidden_rows, "tensor", axis=1, tiled=True),
        flat_weight,
        preferred_element_type=jnp.float32,
    )
    summed = base_out.reshape(row_count, 2, heads_local) + delta_rows.reshape(
        row_count, 2, heads_local
    ).astype(jnp.float32)
    return summed.astype(jnp.bfloat16)


def solution(mesh):
    placed = (
        P("adapter", "tensor"),
        P(None, None, "tensor"),
        P("adapter", "tensor", None),
        P("adapter", None, None, "tensor"),
        P("adapter"),
    )
    return jax.shard_map(
        local, mesh=mesh, in_specs=placed, out_specs=P("adapter", None, "tensor"), check_vma=False
    )
```
